32 devices in a mesh: seq: 8 (over y, x, core), tp: 4 (over z).
Axes of the slice: x: 2, y: 2, z: 4, core: 2. Of those that a mesh axis runs over, the one named last changes fastest.
Arguments:
- projected: bfloat16 [1536, 3, 8192], P('seq', None, 'tp'), may hold values from -6 to 6
- feat_taps: float32 [7, 3, 8192], P(None, None, 'tp'), may hold values from -2.5 to 2.5
- filters: float32 [512, 128], P('tp'), may hold values from -1.5 to 1.5
- out_weight: bfloat16 [8192, 8192], P('tp'), may hold values from -0.09375 to 0.09375
- cotangent: bfloat16 [1536, 8192], P('seq', 'tp'), may hold values from -6 to 6
Outputs:
- output: bfloat16 [1536, 8192], P('seq', 'tp')
- input_grad: bfloat16 [1536, 3, 8192], P('seq', None, 'tp')
The draws below stay inside these ranges and needn't reach their ends.
All inputs are finite; a program needn't handle non-finite values.
Results may differ from the reference program's by a relative error of at most 0.0095.
Values may be sent and summed in bfloat16 or wider, within the bound.
No kernel may reach another device: no remote copies, remote signals or barrier semaphores. Data moves between devices by JAX's collectives and lax.ppermute only.
A program may use at most 128 MiB of HBM per device.

```python
import math
import jax
import jax.numpy as jnp
from jax import lax

D = 8192
FK = 7
FL = 128
HG = 16
GROUPS = 512
TOKENS = 1536
N_TP = 4


def draw_filters(key, part):
    rate_key, tap_key = jax.random.split(jax.random.fold_in(key, 11))
    rates = jnp.exp(jax.random.uniform(rate_key, (GROUPS, 1), jnp.float32, math.log(0.002), math.log(0.1)))
    values = jnp.clip(jax.random.normal(tap_key, (GROUPS, FL), jnp.float32), -6.0, 6.0)
    delays = jnp.arange(FL, dtype=jnp.float32)[None, :]
    return 0.15 * values * jnp.exp(-rates * delays)


def raised(values, stream_key, source, target, blocks, factor):
    owner, partner = [(jnp.arange(values.shape[axis_at]) // (values.shape[axis_at] // blocks)).reshape([-1 if axis == axis_at else 1 for axis in range(values.ndim)]) for axis_at in (source, target)]
    chosen = jax.random.permutation(stream_key, blocks)[partner]
    strong = (owner == chosen) | (owner == (partner + blocks // 2) % blocks)
    return jnp.where(strong, factor * values, values)


def level_of(rng, extent, cuts, least, largest):
    level = 1.0
    for position, parts in cuts:
        draws = jax.random.uniform(jax.random.fold_in(jax.random.fold_in(rng, 6), position), (parts,), jnp.float32, least / len(cuts), largest / len(cuts))
        level = level * jnp.repeat(jnp.exp(draws), extent[position] // parts).reshape((-1,) + (1,) * (len(extent) - 1 - position))
    return level


def bell_draw(key, dims, scale, bound, shards=(), held_as=jnp.bfloat16):
    values = scale * jax.random.normal(key, dims, jnp.float32)
    if shards:
        values = values * level_of(key, dims, shards, -0.22, 0.18)
    return jnp.clip(values, -bound, bound).astype(held_as)


def gaussian_with(stream_key, extent, deviation, limit, shards, heavy, kind=jnp.bfloat16):
    values = deviation * jax.random.normal(stream_key, extent, jnp.float32)
    if shards:
        values = values * level_of(stream_key, extent, shards, -0.22, 0.18)
    return jnp.clip(raised(values, jax.random.fold_in(stream_key, 3), *heavy), -limit, limit).astype(kind)


def setup_inputs(seed: int = 0) -> dict:
    key_list = jax.random.split(jax.random.key(seed), 6)
    return {
        "projected": bell_draw(key_list[0], (TOKENS, 3, D), 1.0, 6.0, ((0, 8), (2, 4))),
        "feat_taps": bell_draw(key_list[1], (FK, 3, D), 0.4, 2.5, ((2, 4),), jnp.float32),
        "filters": draw_filters(jax.random.fold_in(key_list[5], 71), 0),
        "out_weight": gaussian_with(key_list[3], (D, D), D ** -0.5, 0.09375, ((0, 4),), (0, 1, 4, 2.0)),
        "cotangent": bell_draw(key_list[4], (TOKENS, D), 1.0, 6.0, ((0, 8), (1, 4))),
    }


def featurize(signal, feat_weights):
    length = signal.shape[0]
    result = jnp.zeros(signal.shape, jnp.float32)
    for delay in range(feat_weights.shape[0]):
        shifted = jnp.pad(signal[: length - delay], ((delay, 0), (0, 0), (0, 0)))
        result = result + feat_weights[delay] * shifted
    return result


def causal_filter(signal, kernel):
    length = signal.shape[0]
    fft_size = 1 << (length + kernel.shape[1]).bit_length()
    spectrum = jnp.fft.rfft(signal, n=fft_size, axis=0) * jnp.fft.rfft(kernel.T, n=fft_size, axis=0)
    return jnp.fft.irfft(spectrum, n=fft_size, axis=0)[:length].astype(signal.dtype)


def reference(projected, feat_taps, filters, out_weight, cotangent):
    signal = projected.astype(jnp.float32)
    feats = featurize(signal, feat_taps)
    kernel = jnp.repeat(filters, HG, axis=0)
    query = feats[:, 0]
    key_feat = feats[:, 1]
    value_feat = feats[:, 2]
    conv = causal_filter(key_feat * value_feat, kernel)
    mixed = (query * conv).astype(jnp.bfloat16)
    block_width = D // N_TP

    def add_block(block_index, running):
        weight_rows = lax.dynamic_slice_in_dim(out_weight, block_index * block_width, block_width, 0)
        mixed_cols = lax.dynamic_slice_in_dim(mixed, block_index * block_width, block_width, 1)
        partial_sum = jnp.dot(mixed_cols, weight_rows, preferred_element_type=jnp.float32).astype(jnp.bfloat16)
        partial_sum = lax.optimization_barrier(partial_sum)
        return running + partial_sum.astype(jnp.float32)

    summed = lax.fori_loop(0, N_TP, add_block, jnp.zeros((mixed.shape[0], D), jnp.float32))
    output = summed.astype(jnp.bfloat16)
    grad_mixed = jnp.dot(cotangent, out_weight.T, preferred_element_type=jnp.float32)
    signal_grad = grad_mixed * query
    query_grad = grad_mixed * conv
    conv_grad = causal_filter(signal_grad[::-1], kernel)[::-1]
    dfeat = jnp.stack([query_grad, conv_grad * value_feat, conv_grad * key_feat], axis=1)
    length = dfeat.shape[0]
    result = jnp.zeros(dfeat.shape, jnp.float32)
    for delay in range(feat_taps.shape[0]):
        shifted = jnp.pad(dfeat[delay:], ((0, delay), (0, 0), (0, 0)))
        result = result + feat_taps[delay] * shifted
    return output, result.astype(jnp.bfloat16)
```

```python
import jax
import jax.numpy as jnp
from jax import lax
from jax.sharding import PartitionSpec as P


def shift_perm(n, step):
    if step > 0:
        return [(j, j + 1) for j in range(n - 1)]
    return [(j + 1, j) for j in range(n - 1)]


def body(projected, feat_taps, filters, out_weight, cotangent):
    rows = projected.shape[0]
    feat_len = feat_taps.shape[0]
    filt_len = filters.shape[1]
    channels = projected.shape[2]
    group_size = channels // filters.shape[0]
    n = lax.axis_size("seq")
    fwd = shift_perm(n, 1)
    bwd = shift_perm(n, -1)
    fh = feat_len - 1
    lh = filt_len - 1
    assert fh <= rows and lh <= rows

    kern = jnp.repeat(filters, group_size, axis=0).T

    prev_proj = lax.ppermute(projected[rows - fh:], "seq", fwd)
    ext = jnp.concatenate([prev_proj, projected], axis=0).astype(jnp.float32)
    feats = feat_taps[0] * ext[fh:fh + rows]
    for d in range(1, feat_len):
        feats = feats + feat_taps[d] * ext[fh - d:fh - d + rows]
    query = feats[:, 0]
    key_feat = feats[:, 1]
    value_feat = feats[:, 2]
    product = key_feat * value_feat

    prev_prod = lax.ppermute(product[rows - lh:], "seq", fwd)
    pext = jnp.concatenate([prev_prod, product], axis=0)
    conv = kern[0] * pext[lh:lh + rows]
    for d in range(1, filt_len):
        conv = conv + kern[d] * pext[lh - d:lh - d + rows]
    mixed = (query * conv).astype(jnp.bfloat16)

    partial = jnp.einsum(
        "tc,cd->td", mixed, out_weight, preferred_element_type=jnp.float32
    ).astype(jnp.bfloat16)
    output = lax.psum_scatter(partial, "tp", scatter_dimension=1, tiled=True)

    cot_full = lax.all_gather(cotangent, "tp", axis=1, tiled=True)
    grad_mixed = jnp.einsum(
        "te,ce->tc", cot_full, out_weight, preferred_element_type=jnp.float32
    )
    signal_grad = grad_mixed * query
    query_grad = grad_mixed * conv
    next_sig = lax.ppermute(signal_grad[:lh], "seq", bwd)
    sext = jnp.concatenate([signal_grad, next_sig], axis=0)
    conv_grad = kern[0] * sext[:rows]
    for d in range(1, filt_len):
        conv_grad = conv_grad + kern[d] * sext[d:d + rows]
    dfeat = jnp.stack([query_grad, conv_grad * value_feat, conv_grad * key_feat], axis=1)
    next_dfeat = lax.ppermute(dfeat[:fh], "seq", bwd)
    dext = jnp.concatenate([dfeat, next_dfeat], axis=0)
    igrad = feat_taps[0] * dext[:rows]
    for d in range(1, feat_len):
        igrad = igrad + feat_taps[d] * dext[d:d + rows]
    return output, igrad.astype(jnp.bfloat16)


def solution(mesh):
    in_specs = (
        P("seq", None, "tp"),
        P(None, None, "tp"),
        P("tp", None),
        P("tp", None),
        P("seq", "tp"),
    )
    out_specs = (P("seq", "tp"), P("seq", None, "tp"))
    return jax.shard_map(body, mesh=mesh, in_specs=in_specs, out_specs=out_specs, check_vma=False)
```

```python
import jax
import jax.numpy as jnp
from jax import lax
from jax.experimental import pallas as pl
from jax.experimental.pallas import tpu as pltpu
from jax.sharding import PartitionSpec as P

LANES = 128


def _toeplitz_kernel(base_ref, ext_ref, out_ref):
    gb, span = base_ref.shape
    rows, width = out_ref.shape
    hg = width // gb
    p = ext_ref[...]
    p_hi = p.astype(jnp.bfloat16)
    p_lo = (p - p_hi.astype(jnp.float32)).astype(jnp.bfloat16)
    lane_group = lax.broadcasted_iota(jnp.int32, (span, width), 1) // hg
    zero = jnp.zeros_like(p_hi)
    acc = jnp.zeros((rows, width), jnp.float32)
    for g in range(gb):
        t = jnp.broadcast_to(base_ref[pl.ds(g, 1), :], (rows, span))
        t = pltpu.roll(t, 0, 1, stride=1, stride_axis=0)
        t_hi = t.astype(jnp.bfloat16)
        t_lo = (t - t_hi.astype(jnp.float32)).astype(jnp.bfloat16)
        m = lane_group == g
        ph = jnp.where(m, p_hi, zero)
        plo = jnp.where(m, p_lo, zero)
        acc = acc + jnp.dot(t_hi, ph, preferred_element_type=jnp.float32)
        acc = acc + jnp.dot(t_hi, plo, preferred_element_type=jnp.float32)
        acc = acc + jnp.dot(t_lo, ph, preferred_element_type=jnp.float32)
    out_ref[...] = acc


def toeplitz_conv(base, ext, rows):
    groups, span = base.shape
    channels = ext.shape[1]
    gb = groups * LANES // channels
    steps = channels // LANES
    flops = 6 * rows * span * LANES * gb * steps
    return pl.pallas_call(
        _toeplitz_kernel,
        grid=(steps,),
        in_specs=[
            pl.BlockSpec((gb, span), lambda i: (i, 0)),
            pl.BlockSpec((span, LANES), lambda i: (0, i)),
        ],
        out_specs=pl.BlockSpec((rows, LANES), lambda i: (0, i)),
        out_shape=jax.ShapeDtypeStruct((rows, channels), jnp.float32),
        cost_estimate=pl.CostEstimate(
            flops=flops, transcendentals=0,
            bytes_accessed=4 * (base.size + ext.size + rows * channels)),
    )(base, ext)


def shift_perm(n, step):
    if step > 0:
        return [(j, j + 1) for j in range(n - 1)]
    return [(j + 1, j) for j in range(n - 1)]


def body(projected, feat_taps, filters, out_weight, cotangent):
    rows = projected.shape[0]
    feat_len = feat_taps.shape[0]
    filt_len = filters.shape[1]
    channels = projected.shape[2]
    n = lax.axis_size("seq")
    fwd = shift_perm(n, 1)
    bwd = shift_perm(n, -1)
    fh = feat_len - 1
    lh = filt_len - 1
    assert fh <= rows and lh <= rows

    span = -(-(rows + lh) // LANES) * LANES
    tail = span - filt_len
    base_fwd = jnp.pad(filters[:, ::-1], ((0, 0), (0, tail)))
    base_bwd = jnp.pad(filters, ((0, 0), (0, tail)))

    prev_proj = lax.ppermute(projected[rows - fh:], "seq", fwd)
    ext = jnp.concatenate([prev_proj, projected], axis=0).astype(jnp.float32)
    feats = feat_taps[0] * ext[fh:fh + rows]
    for d in range(1, feat_len):
        feats = feats + feat_taps[d] * ext[fh - d:fh - d + rows]
    query = feats[:, 0]
    key_feat = feats[:, 1]
    value_feat = feats[:, 2]
    product = key_feat * value_feat

    prev_prod = lax.ppermute(product[rows - lh:], "seq", fwd)
    pext = jnp.concatenate(
        [prev_prod, product, jnp.zeros((span - rows - lh, channels), jnp.float32)], axis=0
    )
    conv = toeplitz_conv(base_fwd, pext, rows)
    mixed = (query * conv).astype(jnp.bfloat16)

    partial = jnp.einsum(
        "tc,cd->td", mixed, out_weight, preferred_element_type=jnp.float32
    ).astype(jnp.bfloat16)
    output = lax.psum_scatter(partial, "tp", scatter_dimension=1, tiled=True)

    cot_full = lax.all_gather(cotangent, "tp", axis=1, tiled=True)
    grad_mixed = jnp.einsum(
        "te,ce->tc", cot_full, out_weight, preferred_element_type=jnp.float32
    )
    signal_grad = grad_mixed * query
    query_grad = grad_mixed * conv
    next_sig = lax.ppermute(signal_grad[:lh], "seq", bwd)
    sext = jnp.concatenate(
        [signal_grad, next_sig, jnp.zeros((span - rows - lh, channels), jnp.float32)], axis=0
    )
    conv_grad = toeplitz_conv(base_bwd, sext, rows)
    dfeat = jnp.stack([query_grad, conv_grad * value_feat, conv_grad * key_feat], axis=1)
    next_dfeat = lax.ppermute(dfeat[:fh], "seq", bwd)
    dext = jnp.concatenate([dfeat, next_dfeat], axis=0)
    igrad = feat_taps[0] * dext[:rows]
    for d in range(1, feat_len):
        igrad = igrad + feat_taps[d] * dext[d:d + rows]
    return output, igrad.astype(jnp.bfloat16)


def solution(mesh):
    in_specs = (
        P("seq", None, "tp"),
        P(None, None, "tp"),
        P("tp", None),
        P("tp", None),
        P("seq", "tp"),
    )
    out_specs = (P("seq", "tp"), P("seq", None, "tp"))
    return jax.shard_map(body, mesh=mesh, in_specs=in_specs, out_specs=out_specs, check_vma=False)
```

```python
import jax
import jax.numpy as jnp
from jax import lax
from jax.experimental import pallas as pl
from jax.experimental.pallas import tpu as pltpu
from jax.sharding import PartitionSpec as P

LANES = 128


def _toeplitz_kernel(base_ref, ext_ref, out_ref):
    gb, span = base_ref.shape
    rows, width = out_ref.shape
    hg = width // gb
    p = ext_ref[...]
    p_hi = p.astype(jnp.bfloat16)
    p_lo = (p - p_hi.astype(jnp.float32)).astype(jnp.bfloat16)
    lane_group = lax.broadcasted_iota(jnp.int32, (span, width), 1) // hg
    zero = jnp.zeros_like(p_hi)
    acc = jnp.zeros((rows, width), jnp.float32)
    for g in range(gb):
        t = jnp.broadcast_to(base_ref[pl.ds(g, 1), :], (rows, span))
        t = pltpu.roll(t, 0, 1, stride=1, stride_axis=0)
        t_hi = t.astype(jnp.bfloat16)
        t_lo = (t - t_hi.astype(jnp.float32)).astype(jnp.bfloat16)
        m = lane_group == g
        ph = jnp.where(m, p_hi, zero)
        plo = jnp.where(m, p_lo, zero)
        acc = acc + jnp.dot(t_hi, ph, preferred_element_type=jnp.float32)
        acc = acc + jnp.dot(t_hi, plo, preferred_element_type=jnp.float32)
        acc = acc + jnp.dot(t_lo, ph, preferred_element_type=jnp.float32)
    out_ref[...] = acc


def toeplitz_conv(base, ext, rows):
    groups, span = base.shape
    channels = ext.shape[1]
    gb = groups * LANES // channels
    steps = channels // LANES
    flops = 6 * rows * span * LANES * gb * steps
    return pl.pallas_call(
        _toeplitz_kernel,
        grid=(steps,),
        in_specs=[
            pl.BlockSpec((gb, span), lambda i: (i, 0)),
            pl.BlockSpec((span, LANES), lambda i: (0, i)),
        ],
        out_specs=pl.BlockSpec((rows, LANES), lambda i: (0, i)),
        out_shape=jax.ShapeDtypeStruct((rows, channels), jnp.float32),
        cost_estimate=pl.CostEstimate(
            flops=flops, transcendentals=0,
            bytes_accessed=4 * (base.size + ext.size + rows * channels)),
    )(base, ext)


def shift_perm(n, step):
    if step > 0:
        return [(j, j + 1) for j in range(n - 1)]
    return [(j + 1, j) for j in range(n - 1)]


def block(projected, feat_taps, filters, out_weight, cotangent):
    rows = projected.shape[0]
    feat_len = feat_taps.shape[0]
    filt_len = filters.shape[1]
    channels = projected.shape[2]
    n = lax.axis_size("seq")
    fwd = shift_perm(n, 1)
    bwd = shift_perm(n, -1)
    fh = feat_len - 1
    lh = filt_len - 1
    assert fh <= rows and lh <= rows

    span = -(-(rows + lh) // LANES) * LANES
    tail = span - filt_len
    base_fwd = jnp.pad(filters[:, ::-1], ((0, 0), (0, tail)))
    base_bwd = jnp.pad(filters, ((0, 0), (0, tail)))

    prev_proj = lax.ppermute(projected[rows - fh:], "seq", fwd)
    ext = jnp.concatenate([prev_proj, projected], axis=0).astype(jnp.float32)
    feats = feat_taps[0] * ext[fh:fh + rows]
    for d in range(1, feat_len):
        feats = feats + feat_taps[d] * ext[fh - d:fh - d + rows]
    query = feats[:, 0]
    key_feat = feats[:, 1]
    value_feat = feats[:, 2]
    product = key_feat * value_feat

    prev_prod = lax.ppermute(product[rows - lh:], "seq", fwd)
    pext = jnp.concatenate(
        [prev_prod, product, jnp.zeros((span - rows - lh, channels), jnp.float32)], axis=0
    )
    conv = toeplitz_conv(base_fwd, pext, rows)
    mixed = (query * conv).astype(jnp.bfloat16)

    partial = jnp.einsum(
        "tc,cd->td", mixed, out_weight, preferred_element_type=jnp.float32
    ).astype(jnp.bfloat16)
    output = lax.psum_scatter(partial, "tp", scatter_dimension=1, tiled=True)

    query, key_feat, value_feat, conv = lax.optimization_barrier(
        (query, key_feat, value_feat, conv)
    )
    cot_full = lax.all_gather(cotangent, "tp", axis=1, tiled=True)
    grad_mixed = jnp.einsum(
        "te,ce->tc", cot_full, out_weight, preferred_element_type=jnp.float32
    )
    signal_grad = grad_mixed * query
    query_grad = grad_mixed * conv
    next_sig = lax.ppermute(signal_grad[:lh], "seq", bwd)
    sext = jnp.concatenate(
        [signal_grad, next_sig, jnp.zeros((span - rows - lh, channels), jnp.float32)], axis=0
    )
    conv_grad = toeplitz_conv(base_bwd, sext, rows)
    dfeat = jnp.stack([query_grad, conv_grad * value_feat, conv_grad * key_feat], axis=1)
    next_dfeat = lax.ppermute(dfeat[:fh], "seq", bwd)
    dext = jnp.concatenate([dfeat, next_dfeat], axis=0)
    igrad = feat_taps[0] * dext[:rows]
    for d in range(1, feat_len):
        igrad = igrad + feat_taps[d] * dext[d:d + rows]
    return output, igrad.astype(jnp.bfloat16)


def solution(mesh):
    in_specs = (
        P("seq", None, "tp"),
        P(None, None, "tp"),
        P("tp", None),
        P("tp", None),
        P("seq", "tp"),
    )
    out_specs = (P("seq", "tp"), P("seq", None, "tp"))
    return jax.shard_map(block, mesh=mesh, in_specs=in_specs, out_specs=out_specs, check_vma=False)
```

```python
import jax
import jax.numpy as jnp
from jax import lax
from jax.experimental import pallas as pl
from jax.experimental.pallas import tpu as pltpu
from jax.sharding import PartitionSpec as P

LANES = 128


def _toeplitz_kernel(base_ref, ext_ref, out_ref):
    gb, span = base_ref.shape
    rows, width = out_ref.shape
    half = rows // 2
    hg = width // gb
    p = ext_ref[...]
    p2 = jnp.concatenate([p[:span], p[half:half + span]], axis=1)
    p_hi = p2.astype(jnp.bfloat16)
    p_lo = (p2 - p_hi.astype(jnp.float32)).astype(jnp.bfloat16)
    lane_group = (lax.broadcasted_iota(jnp.int32, (half, 2 * width), 1) % width) // hg
    acc = jnp.zeros((half, 2 * width), jnp.float32)
    for g in range(gb):
        t = jnp.broadcast_to(base_ref[pl.ds(g, 1), :], (half, span))
        t = pltpu.roll(t, 0, 1, stride=1, stride_axis=0).astype(jnp.bfloat16)
        res = jnp.dot(t, p_hi, preferred_element_type=jnp.float32)
        res = res + jnp.dot(t, p_lo, preferred_element_type=jnp.float32)
        acc = jnp.where(lane_group == g, res, acc)
    out_ref[pl.ds(0, half), :] = acc[:, :width]
    out_ref[pl.ds(half, half), :] = acc[:, width:]


def toeplitz_conv(base, ext, rows):
    groups, span = base.shape
    length, channels = ext.shape
    half = rows // 2
    assert rows % 32 == 0 and half + span <= length and span >= half + LANES - 1
    gb = groups * LANES // channels
    steps = channels // LANES
    flops = 4 * half * span * 2 * LANES * gb * steps
    return pl.pallas_call(
        _toeplitz_kernel,
        grid=(steps,),
        in_specs=[
            pl.BlockSpec((gb, span), lambda i: (i, 0)),
            pl.BlockSpec((length, LANES), lambda i: (0, i)),
        ],
        out_specs=pl.BlockSpec((rows, LANES), lambda i: (0, i)),
        out_shape=jax.ShapeDtypeStruct((rows, channels), jnp.float32),
        cost_estimate=pl.CostEstimate(
            flops=flops, transcendentals=0,
            bytes_accessed=4 * (base.size + ext.size + rows * channels)),
    )(base, ext)


def shift_perm(n, step):
    if step > 0:
        return [(j, j + 1) for j in range(n - 1)]
    return [(j + 1, j) for j in range(n - 1)]


def block(projected, feat_taps, filters, out_weight, cotangent):
    rows = projected.shape[0]
    feat_len = feat_taps.shape[0]
    filt_len = filters.shape[1]
    channels = projected.shape[2]
    n = lax.axis_size("seq")
    fwd = shift_perm(n, 1)
    bwd = shift_perm(n, -1)
    fh = feat_len - 1
    lh = filt_len - 1
    reach = lh + fh
    assert reach <= rows
    ext_len = -(-(rows + reach) // LANES) * LANES
    fwd_rows = rows
    bwd_rows = -(-(rows + fh) // 32) * 32
    span_f = -(-(fwd_rows // 2 + lh) // LANES) * LANES
    span_b = -(-(bwd_rows // 2 + lh) // LANES) * LANES
    base_fwd = jnp.pad(filters[:, ::-1], ((0, 0), (0, span_f - filt_len))).astype(jnp.bfloat16)
    base_bwd = jnp.pad(filters, ((0, 0), (0, span_b - filt_len))).astype(jnp.bfloat16)
    base_fwd = base_fwd.astype(jnp.float32)
    base_bwd = base_bwd.astype(jnp.float32)

    prev_proj = lax.ppermute(projected[rows - fh:], "seq", fwd)
    next_proj = lax.ppermute(projected[:fh], "seq", bwd)
    ext = jnp.concatenate([prev_proj, projected, next_proj], axis=0).astype(jnp.float32)
    feats = feat_taps[0] * ext[fh:fh + rows + fh]
    for d in range(1, feat_len):
        feats = feats + feat_taps[d] * ext[fh - d:fh - d + rows + fh]
    query = feats[:rows, 0]
    key_ext = feats[:, 1]
    value_ext = feats[:, 2]
    key_feat = key_ext[:rows]
    value_feat = value_ext[:rows]
    product = key_feat * value_feat

    prev_prod = lax.ppermute(product[rows - lh:], "seq", fwd)
    pext = jnp.concatenate(
        [prev_prod, product, jnp.zeros((ext_len - rows - lh, channels), jnp.float32)], axis=0
    )
    conv = toeplitz_conv(base_fwd, pext, fwd_rows)
    mixed = (query * conv).astype(jnp.bfloat16)

    partial = jnp.einsum(
        "tc,cd->td", mixed, out_weight, preferred_element_type=jnp.float32
    ).astype(jnp.bfloat16)
    output = lax.psum_scatter(partial, "tp", scatter_dimension=1, tiled=True)

    query, key_ext, value_ext, conv = lax.optimization_barrier(
        (query, key_ext, value_ext, conv)
    )
    cot_full = lax.all_gather(cotangent, "tp", axis=1, tiled=True)
    grad_mixed = jnp.einsum(
        "te,ce->tc", cot_full, out_weight, preferred_element_type=jnp.float32
    )
    signal_grad = grad_mixed * query
    query_grad = grad_mixed * conv
    next_sig, next_qg = lax.ppermute((signal_grad[:reach], query_grad[:fh]), "seq", bwd)
    sext = jnp.concatenate(
        [signal_grad, next_sig, jnp.zeros((ext_len - rows - reach, channels), jnp.float32)], axis=0
    )
    conv_grad = toeplitz_conv(base_bwd, sext, bwd_rows)[:rows + fh]
    qg_ext = jnp.concatenate([query_grad, next_qg], axis=0)
    dext = jnp.stack([qg_ext, conv_grad * value_ext, conv_grad * key_ext], axis=1)
    igrad = feat_taps[0] * dext[:rows]
    for d in range(1, feat_len):
        igrad = igrad + feat_taps[d] * dext[d:d + rows]
    return output, igrad.astype(jnp.bfloat16)


def solution(mesh):
    in_specs = (
        P("seq", None, "tp"),
        P(None, None, "tp"),
        P("tp", None),
        P("tp", None),
        P("seq", "tp"),
    )
    out_specs = (P("seq", "tp"), P("seq", None, "tp"))
    return jax.shard_map(block, mesh=mesh, in_specs=in_specs, out_specs=out_specs, check_vma=False)
```

```python
import jax
import jax.numpy as jnp
from jax import lax
from jax.experimental import pallas as pl
from jax.experimental.pallas import tpu as pltpu
from jax.sharding import PartitionSpec as P

LANES = 128


def _toeplitz_kernel(base_ref, ext_ref, out_ref):
    gb, span = base_ref.shape
    rows, width = out_ref.shape
    half = rows // 2
    hg = width // gb
    p = ext_ref[...]
    p2 = jnp.concatenate([p[:span], p[half:half + span]], axis=1)
    p_hi = p2.astype(jnp.bfloat16)
    p_lo = (p2 - p_hi.astype(jnp.float32)).astype(jnp.bfloat16)
    lane_group = (lax.broadcasted_iota(jnp.int32, (half, 2 * width), 1) % width) // hg
    acc = jnp.zeros((half, 2 * width), jnp.float32)
    for g in range(gb):
        t = jnp.broadcast_to(base_ref[pl.ds(g, 1), :], (half, span))
        t = pltpu.roll(t, 0, 1, stride=1, stride_axis=0)
        t_hi = t.astype(jnp.bfloat16)
        t_lo = (t - t_hi.astype(jnp.float32)).astype(jnp.bfloat16)
        res = jnp.dot(t_hi, p_hi, preferred_element_type=jnp.float32)
        res = res + jnp.dot(t_hi, p_lo, preferred_element_type=jnp.float32)
        res = res + jnp.dot(t_lo, p_hi, preferred_element_type=jnp.float32)
        acc = jnp.where(lane_group == g, res, acc)
    out_ref[pl.ds(0, half), :] = acc[:, :width]
    out_ref[pl.ds(half, half), :] = acc[:, width:]


def toeplitz_conv(base, ext, rows):
    groups, span = base.shape
    length, channels = ext.shape
    half = rows // 2
    assert rows % 32 == 0 and half + span <= length and span >= half + LANES - 1
    gb = groups * LANES // channels
    steps = channels // LANES
    flops = 6 * half * span * 2 * LANES * gb * steps
    return pl.pallas_call(
        _toeplitz_kernel,
        grid=(steps,),
        in_specs=[
            pl.BlockSpec((gb, span), lambda i: (i, 0)),
            pl.BlockSpec((length, LANES), lambda i: (0, i)),
        ],
        out_specs=pl.BlockSpec((rows, LANES), lambda i: (0, i)),
        out_shape=jax.ShapeDtypeStruct((rows, channels), jnp.float32),
        cost_estimate=pl.CostEstimate(
            flops=flops, transcendentals=0,
            bytes_accessed=4 * (base.size + ext.size + rows * channels)),
    )(base, ext)


def shift_perm(n, step):
    if step > 0:
        return [(j, j + 1) for j in range(n - 1)]
    return [(j + 1, j) for j in range(n - 1)]


def block(projected, feat_taps, filters, out_weight, cotangent):
    rows = projected.shape[0]
    feat_len = feat_taps.shape[0]
    filt_len = filters.shape[1]
    channels = projected.shape[2]
    n = lax.axis_size("seq")
    fwd = shift_perm(n, 1)
    bwd = shift_perm(n, -1)
    fh = feat_len - 1
    lh = filt_len - 1
    reach = lh + fh
    assert reach <= rows
    ext_len = -(-(rows + reach) // LANES) * LANES
    fwd_rows = rows
    bwd_rows = -(-(rows + fh) // 32) * 32
    span_f = -(-(fwd_rows // 2 + lh) // LANES) * LANES
    span_b = -(-(bwd_rows // 2 + lh) // LANES) * LANES
    base_fwd = jnp.pad(filters[:, ::-1], ((0, 0), (0, span_f - filt_len)))
    base_bwd = jnp.pad(filters, ((0, 0), (0, span_b - filt_len)))

    prev_proj = lax.ppermute(projected[rows - fh:], "seq", fwd)
    next_proj = lax.ppermute(projected[:fh], "seq", bwd)
    ext = jnp.concatenate([prev_proj, projected, next_proj], axis=0).astype(jnp.float32)
    feats = feat_taps[0] * ext[fh:fh + rows + fh]
    for d in range(1, feat_len):
        feats = feats + feat_taps[d] * ext[fh - d:fh - d + rows + fh]
    query = feats[:rows, 0]
    key_ext = feats[:, 1]
    value_ext = feats[:, 2]
    key_feat = key_ext[:rows]
    value_feat = value_ext[:rows]
    product = key_feat * value_feat

    prev_prod = lax.ppermute(product[rows - lh:], "seq", fwd)
    pext = jnp.concatenate(
        [prev_prod, product, jnp.zeros((ext_len - rows - lh, channels), jnp.float32)], axis=0
    )
    conv = toeplitz_conv(base_fwd, pext, fwd_rows)
    mixed = (query * conv).astype(jnp.bfloat16)

    partial = jnp.einsum(
        "tc,cd->td", mixed, out_weight, preferred_element_type=jnp.float32
    ).astype(jnp.bfloat16)
    output = lax.psum_scatter(partial, "tp", scatter_dimension=1, tiled=True)

    query, key_ext, value_ext, conv = lax.optimization_barrier(
        (query, key_ext, value_ext, conv)
    )
    cot_full = lax.all_gather(cotangent, "tp", axis=1, tiled=True)
    grad_mixed = jnp.einsum(
        "te,ce->tc", cot_full, out_weight, preferred_element_type=jnp.float32
    )
    signal_grad = grad_mixed * query
    query_grad = grad_mixed * conv
    next_sig, next_qg = lax.ppermute((signal_grad[:reach], query_grad[:fh]), "seq", bwd)
    sext = jnp.concatenate(
        [signal_grad, next_sig, jnp.zeros((ext_len - rows - reach, channels), jnp.float32)], axis=0
    )
    conv_grad = toeplitz_conv(base_bwd, sext, bwd_rows)[:rows + fh]
    qg_ext = jnp.concatenate([query_grad, next_qg], axis=0)
    dext = jnp.stack([qg_ext, conv_grad * value_ext, conv_grad * key_ext], axis=1)
    igrad = feat_taps[0] * dext[:rows]
    for d in range(1, feat_len):
        igrad = igrad + feat_taps[d] * dext[d:d + rows]
    return output, igrad.astype(jnp.bfloat16)


def solution(mesh):
    in_specs = (
        P("seq", None, "tp"),
        P(None, None, "tp"),
        P("tp", None),
        P("tp", None),
        P("seq", "tp"),
    )
    out_specs = (P("seq", "tp"), P("seq", None, "tp"))
    return jax.shard_map(block, mesh=mesh, in_specs=in_specs, out_specs=out_specs, check_vma=False)
```

```python
import jax
import jax.numpy as jnp
from jax import lax
from jax.experimental import pallas as pl
from jax.experimental.pallas import tpu as pltpu
from jax.sharding import PartitionSpec as P

LANES = 128


def _toeplitz_kernel(base_ref, ext_ref, out_ref):
    gb, span = base_ref.shape
    rows, width = out_ref.shape
    half = rows // 2
    hg = width // gb
    p = ext_ref[...]
    p2 = jnp.concatenate([p[:span], p[half:half + span]], axis=1)
    p_hi = p2.astype(jnp.bfloat16)
    p_lo = (p2 - p_hi.astype(jnp.float32)).astype(jnp.bfloat16)
    lane_group = (lax.broadcasted_iota(jnp.int32, (half, 2 * width), 1) % width) // hg
    acc = jnp.zeros((half, 2 * width), jnp.float32)
    for g in range(gb):
        t = jnp.broadcast_to(base_ref[pl.ds(g, 1), :], (half, span))
        t = pltpu.roll(t, 0, 1, stride=1, stride_axis=0).astype(jnp.bfloat16)
        res = jnp.dot(t, p_hi, preferred_element_type=jnp.float32)
        res = res + jnp.dot(t, p_lo, preferred_element_type=jnp.float32)
        acc = jnp.where(lane_group == g, res, acc)
    out_ref[pl.ds(0, half), :] = acc[:, :width]
    out_ref[pl.ds(half, half), :] = acc[:, width:]


def toeplitz_conv(base, ext, rows):
    groups, span = base.shape
    length, channels = ext.shape
    half = rows // 2
    assert rows % 32 == 0 and half + span <= length and span >= half + LANES - 1
    gb = groups * LANES // channels
    steps = channels // LANES
    flops = 4 * half * span * 2 * LANES * gb * steps
    return pl.pallas_call(
        _toeplitz_kernel,
        grid=(steps,),
        in_specs=[
            pl.BlockSpec((gb, span), lambda i: (i, 0)),
            pl.BlockSpec((length, LANES), lambda i: (0, i)),
        ],
        out_specs=pl.BlockSpec((rows, LANES), lambda i: (0, i)),
        out_shape=jax.ShapeDtypeStruct((rows, channels), jnp.float32),
        cost_estimate=pl.CostEstimate(
            flops=flops, transcendentals=0,
            bytes_accessed=4 * (base.size + ext.size + rows * channels)),
    )(base, ext)


def shift_perm(n, step):
    if step > 0:
        return [(j, j + 1) for j in range(n - 1)]
    return [(j + 1, j) for j in range(n - 1)]


def tp_reduce_scatter(part, axis_name):
    n = lax.axis_size(axis_name)
    if n > 8:
        return lax.psum_scatter(part, axis_name, scatter_dimension=1, tiled=True)
    k = lax.axis_index(axis_name)
    width = part.shape[1] // n
    recv_r = jnp.zeros((part.shape[0], width), part.dtype)
    recv_l = recv_r
    for s in range(1, n):
        blk_r = lax.dynamic_slice_in_dim(part, (k + n - s) * width, width, axis=1)
        blk_l = lax.dynamic_slice_in_dim(part, jnp.maximum(k - (n - s), 0) * width, width, axis=1)
        msg_r = (blk_r.astype(jnp.float32) + recv_r.astype(jnp.float32)).astype(part.dtype)
        msg_l = (blk_l.astype(jnp.float32) + recv_l.astype(jnp.float32)).astype(part.dtype)
        recv_r = lax.ppermute(msg_r, axis_name, [(j, j + 1) for j in range(0, s)])
        recv_l = lax.ppermute(msg_l, axis_name, [(j, j - 1) for j in range(n - s, n)])
    own = lax.dynamic_slice_in_dim(part, k * width, width, axis=1)
    total = own.astype(jnp.float32) + recv_r.astype(jnp.float32) + recv_l.astype(jnp.float32)
    return total.astype(part.dtype)


def block(projected, feat_taps, filters, out_weight, cotangent):
    rows = projected.shape[0]
    feat_len = feat_taps.shape[0]
    filt_len = filters.shape[1]
    channels = projected.shape[2]
    n = lax.axis_size("seq")
    fwd = shift_perm(n, 1)
    bwd = shift_perm(n, -1)
    fh = feat_len - 1
    lh = filt_len - 1
    reach = lh + fh
    assert reach <= rows
    ext_len = -(-(rows + reach) // LANES) * LANES
    fwd_rows = rows
    bwd_rows = -(-(rows + fh) // 32) * 32
    span_f = -(-(fwd_rows // 2 + lh) // LANES) * LANES
    span_b = -(-(bwd_rows // 2 + lh) // LANES) * LANES
    base_fwd = jnp.pad(filters[:, ::-1], ((0, 0), (0, span_f - filt_len))).astype(jnp.bfloat16)
    base_bwd = jnp.pad(filters, ((0, 0), (0, span_b - filt_len))).astype(jnp.bfloat16)
    base_fwd = base_fwd.astype(jnp.float32)
    base_bwd = base_bwd.astype(jnp.float32)

    prev_proj = lax.ppermute(projected[rows - fh:], "seq", fwd)
    next_proj = lax.ppermute(projected[:fh], "seq", bwd)
    ext = jnp.concatenate([prev_proj, projected, next_proj], axis=0).astype(jnp.float32)
    feats = feat_taps[0] * ext[fh:fh + rows + fh]
    for d in range(1, feat_len):
        feats = feats + feat_taps[d] * ext[fh - d:fh - d + rows + fh]
    query = feats[:rows, 0]
    key_ext = feats[:, 1]
    value_ext = feats[:, 2]
    key_feat = key_ext[:rows]
    value_feat = value_ext[:rows]
    product = key_feat * value_feat

    prev_prod = lax.ppermute(product[rows - lh:], "seq", fwd)
    pext = jnp.concatenate(
        [prev_prod, product, jnp.zeros((ext_len - rows - lh, channels), jnp.float32)], axis=0
    )
    conv = toeplitz_conv(base_fwd, pext, fwd_rows)
    mixed = (query * conv).astype(jnp.bfloat16)

    partial = jnp.einsum(
        "tc,cd->td", mixed, out_weight, preferred_element_type=jnp.float32
    ).astype(jnp.bfloat16)
    output = tp_reduce_scatter(partial, "tp")

    query, key_ext, value_ext, conv = lax.optimization_barrier(
        (query, key_ext, value_ext, conv)
    )
    cot_full = lax.all_gather(cotangent, "tp", axis=1, tiled=True)
    grad_mixed = jnp.einsum("te,ce->tc", cot_full, out_weight, preferred_element_type=jnp.float32)
    signal_grad = grad_mixed * query
    query_grad = grad_mixed * conv
    next_sig, next_qg = lax.ppermute((signal_grad[:reach], query_grad[:fh]), "seq", bwd)
    sext = jnp.concatenate(
        [signal_grad, next_sig, jnp.zeros((ext_len - rows - reach, channels), jnp.float32)], axis=0
    )
    conv_grad = toeplitz_conv(base_bwd, sext, bwd_rows)[:rows + fh]
    qg_ext = jnp.concatenate([query_grad, next_qg], axis=0)
    dext = jnp.stack([qg_ext, conv_grad * value_ext, conv_grad * key_ext], axis=1)
    igrad = feat_taps[0] * dext[:rows]
    for d in range(1, feat_len):
        igrad = igrad + feat_taps[d] * dext[d:d + rows]
    return output, igrad.astype(jnp.bfloat16)


def solution(mesh):
    in_specs = (
        P("seq", None, "tp"),
        P(None, None, "tp"),
        P("tp", None),
        P("tp", None),
        P("seq", "tp"),
    )
    out_specs = (P("seq", "tp"), P("seq", None, "tp"))
    return jax.shard_map(block, mesh=mesh, in_specs=in_specs, out_specs=out_specs, check_vma=False)
```

```python
import jax
import jax.numpy as jnp
from jax import lax
from jax.experimental import pallas as pl
from jax.experimental.pallas import tpu as pltpu
from jax.sharding import PartitionSpec as P

LANES = 128


def _toeplitz_kernel(base_ref, ext_ref, out_ref):
    gb, span = base_ref.shape
    rows, width = out_ref.shape
    half = rows // 2
    hg = width // gb
    p = ext_ref[...]
    p2 = jnp.concatenate([p[:span], p[half:half + span]], axis=1)
    p_hi = p2.astype(jnp.bfloat16)
    p_lo = (p2 - p_hi.astype(jnp.float32)).astype(jnp.bfloat16)
    lane_group = (lax.broadcasted_iota(jnp.int32, (half, 2 * width), 1) % width) // hg
    acc = jnp.zeros((half, 2 * width), jnp.float32)
    for g in range(gb):
        t = jnp.broadcast_to(base_ref[pl.ds(g, 1), :], (half, span))
        t = pltpu.roll(t, 0, 1, stride=1, stride_axis=0).astype(jnp.bfloat16)
        res = jnp.dot(t, p_hi, preferred_element_type=jnp.float32)
        res = res + jnp.dot(t, p_lo, preferred_element_type=jnp.float32)
        acc = jnp.where(lane_group == g, res, acc)
    out_ref[pl.ds(0, half), :] = acc[:, :width]
    out_ref[pl.ds(half, half), :] = acc[:, width:]


def toeplitz_conv(base, ext, rows):
    groups, span = base.shape
    length, channels = ext.shape
    half = rows // 2
    assert rows % 32 == 0 and half + span <= length and span >= half + LANES - 1
    gb = groups * LANES // channels
    steps = channels // LANES
    flops = 4 * half * span * 2 * LANES * gb * steps
    return pl.pallas_call(
        _toeplitz_kernel,
        grid=(steps,),
        in_specs=[
            pl.BlockSpec((gb, span), lambda i: (i, 0)),
            pl.BlockSpec((length, LANES), lambda i: (0, i)),
        ],
        out_specs=pl.BlockSpec((rows, LANES), lambda i: (0, i)),
        out_shape=jax.ShapeDtypeStruct((rows, channels), jnp.float32),
        cost_estimate=pl.CostEstimate(
            flops=flops, transcendentals=0,
            bytes_accessed=4 * (base.size + ext.size + rows * channels)),
    )(base, ext)


def shift_perm(n, step):
    if step > 0:
        return [(j, j + 1) for j in range(n - 1)]
    return [(j + 1, j) for j in range(n - 1)]


def tp_all_gather(x, axis_name):
    n = lax.axis_size(axis_name)
    if n > 8:
        return lax.all_gather(x, axis_name, axis=1, tiled=True)
    k = lax.axis_index(axis_name)
    width = x.shape[1]
    right = x
    left = x
    got_r = []
    got_l = []
    for s in range(1, n):
        right = lax.ppermute(right, axis_name, [(j, j + 1) for j in range(s - 1, n - 1)])
        left = lax.ppermute(left, axis_name, [(j + 1, j) for j in range(0, n - s)])
        got_r.append(right)
        got_l.append(left)
    stacked = jnp.concatenate(got_r[::-1] + [x] + got_l, axis=1)
    return lax.dynamic_slice_in_dim(stacked, (n - 1 - k) * width, n * width, axis=1)


def block(projected, feat_taps, filters, out_weight, cotangent):
    rows = projected.shape[0]
    feat_len = feat_taps.shape[0]
    filt_len = filters.shape[1]
    channels = projected.shape[2]
    n = lax.axis_size("seq")
    fwd = shift_perm(n, 1)
    bwd = shift_perm(n, -1)
    fh = feat_len - 1
    lh = filt_len - 1
    reach = lh + fh
    assert reach <= rows
    ext_len = -(-(rows + reach) // LANES) * LANES
    fwd_rows = rows
    bwd_rows = -(-(rows + fh) // 32) * 32
    span_f = -(-(fwd_rows // 2 + lh) // LANES) * LANES
    span_b = -(-(bwd_rows // 2 + lh) // LANES) * LANES
    base_fwd = jnp.pad(filters[:, ::-1], ((0, 0), (0, span_f - filt_len))).astype(jnp.bfloat16)
    base_bwd = jnp.pad(filters, ((0, 0), (0, span_b - filt_len))).astype(jnp.bfloat16)
    base_fwd = base_fwd.astype(jnp.float32)
    base_bwd = base_bwd.astype(jnp.float32)

    prev_proj = lax.ppermute(projected[rows - fh:], "seq", fwd)
    next_proj = lax.ppermute(projected[:fh], "seq", bwd)
    ext = jnp.concatenate([prev_proj, projected, next_proj], axis=0).astype(jnp.float32)
    feats = feat_taps[0] * ext[fh:fh + rows + fh]
    for d in range(1, feat_len):
        feats = feats + feat_taps[d] * ext[fh - d:fh - d + rows + fh]
    query = feats[:rows, 0]
    key_ext = feats[:, 1]
    value_ext = feats[:, 2]
    key_feat = key_ext[:rows]
    value_feat = value_ext[:rows]
    product = key_feat * value_feat

    prev_prod = lax.ppermute(product[rows - lh:], "seq", fwd)
    pext = jnp.concatenate(
        [prev_prod, product, jnp.zeros((ext_len - rows - lh, channels), jnp.float32)], axis=0
    )
    conv = toeplitz_conv(base_fwd, pext, fwd_rows)
    mixed = (query * conv).astype(jnp.bfloat16)

    partial = jnp.einsum(
        "tc,cd->td", mixed, out_weight, preferred_element_type=jnp.float32
    ).astype(jnp.bfloat16)
    output = lax.psum_scatter(partial, "tp", scatter_dimension=1, tiled=True)

    query, key_ext, value_ext, conv = lax.optimization_barrier(
        (query, key_ext, value_ext, conv)
    )
    cot_full = tp_all_gather(cotangent, "tp")
    grad_mixed = jnp.einsum(
        "te,ce->tc", cot_full, out_weight, preferred_element_type=jnp.float32
    )
    signal_grad = grad_mixed * query
    query_grad = grad_mixed * conv
    next_sig, next_qg = lax.ppermute((signal_grad[:reach], query_grad[:fh]), "seq", bwd)
    sext = jnp.concatenate(
        [signal_grad, next_sig, jnp.zeros((ext_len - rows - reach, channels), jnp.float32)], axis=0
    )
    conv_grad = toeplitz_conv(base_bwd, sext, bwd_rows)[:rows + fh]
    qg_ext = jnp.concatenate([query_grad, next_qg], axis=0)
    dext = jnp.stack([qg_ext, conv_grad * value_ext, conv_grad * key_ext], axis=1)
    igrad = feat_taps[0] * dext[:rows]
    for d in range(1, feat_len):
        igrad = igrad + feat_taps[d] * dext[d:d + rows]
    return output, igrad.astype(jnp.bfloat16)


def solution(mesh):
    in_specs = (
        P("seq", None, "tp"),
        P(None, None, "tp"),
        P("tp", None),
        P("tp", None),
        P("seq", "tp"),
    )
    out_specs = (P("seq", "tp"), P("seq", None, "tp"))
    return jax.shard_map(block, mesh=mesh, in_specs=in_specs, out_specs=out_specs, check_vma=False)
```

```python
import jax
import jax.numpy as jnp
from jax import lax
from jax.experimental import pallas as pl
from jax.experimental.pallas import tpu as pltpu
from jax.sharding import PartitionSpec as P

LANES = 128


def _toeplitz_kernel(base_ref, ext_ref, out_ref):
    gb, span = base_ref.shape
    rows, width = out_ref.shape
    half = rows // 2
    hg = width // gb
    p = ext_ref[...]
    p2 = jnp.concatenate([p[:span], p[half:half + span]], axis=1)
    p_hi = p2.astype(jnp.bfloat16)
    p_lo = (p2 - p_hi.astype(jnp.float32)).astype(jnp.bfloat16)
    lane_group = (lax.broadcasted_iota(jnp.int32, (half, 2 * width), 1) % width) // hg
    acc = jnp.zeros((half, 2 * width), jnp.float32)
    for g in range(gb):
        t = jnp.broadcast_to(base_ref[pl.ds(g, 1), :], (half, span))
        t = pltpu.roll(t, 0, 1, stride=1, stride_axis=0).astype(jnp.bfloat16)
        res = jnp.dot(t, p_hi, preferred_element_type=jnp.float32)
        res = res + jnp.dot(t, p_lo, preferred_element_type=jnp.float32)
        acc = jnp.where(lane_group == g, res, acc)
    out_ref[pl.ds(0, half), :] = acc[:, :width]
    out_ref[pl.ds(half, half), :] = acc[:, width:]


def toeplitz_conv(base, ext, rows):
    groups, span = base.shape
    length, channels = ext.shape
    half = rows // 2
    assert rows % 32 == 0 and half + span <= length and span >= half + LANES - 1
    gb = groups * LANES // channels
    steps = channels // LANES
    flops = 4 * half * span * 2 * LANES * gb * steps
    return pl.pallas_call(
        _toeplitz_kernel,
        grid=(steps,),
        in_specs=[
            pl.BlockSpec((gb, span), lambda i: (i, 0)),
            pl.BlockSpec((length, LANES), lambda i: (0, i)),
        ],
        out_specs=pl.BlockSpec((rows, LANES), lambda i: (0, i)),
        out_shape=jax.ShapeDtypeStruct((rows, channels), jnp.float32),
        cost_estimate=pl.CostEstimate(
            flops=flops, transcendentals=0,
            bytes_accessed=4 * (base.size + ext.size + rows * channels)),
    )(base, ext)


def shift_perm(n, step):
    if step > 0:
        return [(j, j + 1) for j in range(n - 1)]
    return [(j + 1, j) for j in range(n - 1)]


def block(projected, feat_taps, filters, out_weight, cotangent):
    rows = projected.shape[0]
    feat_len = feat_taps.shape[0]
    filt_len = filters.shape[1]
    channels = projected.shape[2]
    n = lax.axis_size("seq")
    fwd = shift_perm(n, 1)
    bwd = shift_perm(n, -1)
    fh = feat_len - 1
    lh = filt_len - 1
    reach = lh + fh
    assert reach <= rows
    ext_len = -(-(rows + reach) // LANES) * LANES
    fwd_rows = rows
    bwd_rows = -(-(rows + fh) // 32) * 32
    span_f = -(-(fwd_rows // 2 + lh) // LANES) * LANES
    span_b = -(-(bwd_rows // 2 + lh) // LANES) * LANES
    base_fwd = jnp.pad(filters[:, ::-1], ((0, 0), (0, span_f - filt_len))).astype(jnp.bfloat16)
    base_bwd = jnp.pad(filters, ((0, 0), (0, span_b - filt_len))).astype(jnp.bfloat16)
    base_fwd = base_fwd.astype(jnp.float32)
    base_bwd = base_bwd.astype(jnp.float32)

    prev_proj = lax.ppermute(projected[rows - fh:], "seq", fwd)
    next_proj = lax.ppermute(projected[:fh], "seq", bwd)
    ext = jnp.concatenate([prev_proj, projected, next_proj], axis=0)

    def featurize(stream, out_rows):
        sig = ext[:, stream].astype(jnp.float32)
        out = feat_taps[0, stream] * sig[fh:fh + out_rows]
        for d in range(1, feat_len):
            out = out + feat_taps[d, stream] * sig[fh - d:fh - d + out_rows]
        return out

    query = featurize(0, rows)
    key_ext = featurize(1, rows + fh)
    value_ext = featurize(2, rows + fh)
    key_feat = key_ext[:rows]
    value_feat = value_ext[:rows]
    product = key_feat * value_feat

    prev_prod = lax.ppermute(product[rows - lh:], "seq", fwd)
    pext = jnp.concatenate(
        [prev_prod, product, jnp.zeros((ext_len - rows - lh, channels), jnp.float32)], axis=0
    )
    conv = toeplitz_conv(base_fwd, pext, fwd_rows)
    mixed = (query * conv).astype(jnp.bfloat16)

    partial = jnp.einsum(
        "tc,cd->td", mixed, out_weight, preferred_element_type=jnp.float32
    ).astype(jnp.bfloat16)
    output = lax.psum_scatter(partial, "tp", scatter_dimension=1, tiled=True)

    query, key_ext, value_ext, conv = lax.optimization_barrier(
        (query, key_ext, value_ext, conv)
    )
    cot_full = lax.all_gather(cotangent, "tp", axis=1, tiled=True)
    grad_mixed = jnp.einsum(
        "te,ce->tc", cot_full, out_weight, preferred_element_type=jnp.float32
    )
    signal_grad = grad_mixed * query
    query_grad = grad_mixed * conv
    next_sig, next_qg = lax.ppermute((signal_grad[:reach], query_grad[:fh]), "seq", bwd)
    sext = jnp.concatenate(
        [signal_grad, next_sig, jnp.zeros((ext_len - rows - reach, channels), jnp.float32)], axis=0
    )
    conv_grad = toeplitz_conv(base_bwd, sext, bwd_rows)[:rows + fh]
    qg_ext = jnp.concatenate([query_grad, next_qg], axis=0)
    dext = jnp.stack([qg_ext, conv_grad * value_ext, conv_grad * key_ext], axis=1)
    igrad = feat_taps[0] * dext[:rows]
    for d in range(1, feat_len):
        igrad = igrad + feat_taps[d] * dext[d:d + rows]
    return output, igrad.astype(jnp.bfloat16)


def solution(mesh):
    in_specs = (
        P("seq", None, "tp"),
        P(None, None, "tp"),
        P("tp", None),
        P("tp", None),
        P("seq", "tp"),
    )
    out_specs = (P("seq", "tp"), P("seq", None, "tp"))
    return jax.shard_map(block, mesh=mesh, in_specs=in_specs, out_specs=out_specs, check_vma=False)
```

```python
import jax
import jax.numpy as jnp
from jax import lax
from jax.experimental import pallas as pl
from jax.experimental.pallas import tpu as pltpu
from jax.sharding import PartitionSpec as P

LANES = 128


def _toeplitz_kernel(base_ref, ext_ref, out_ref):
    gb, span = base_ref.shape
    rows, width = out_ref.shape
    half = rows // 2
    hg = width // gb
    p = ext_ref[...]
    p2 = jnp.concatenate([p[:span], p[half:half + span]], axis=1)
    p_hi = p2.astype(jnp.bfloat16)
    p_lo = (p2 - p_hi.astype(jnp.float32)).astype(jnp.bfloat16)
    lane_group = (lax.broadcasted_iota(jnp.int32, (half, 2 * width), 1) % width) // hg
    acc = jnp.zeros((half, 2 * width), jnp.float32)
    for g in range(gb):
        t = jnp.broadcast_to(base_ref[pl.ds(g, 1), :], (half, span))
        t = pltpu.roll(t, 0, 1, stride=1, stride_axis=0).astype(jnp.bfloat16)
        res = jnp.dot(t, p_hi, preferred_element_type=jnp.float32)
        res = res + jnp.dot(t, p_lo, preferred_element_type=jnp.float32)
        acc = jnp.where(lane_group == g, res, acc)
    out_ref[pl.ds(0, half), :] = acc[:, :width]
    out_ref[pl.ds(half, half), :] = acc[:, width:]


def toeplitz_conv(base, ext, rows):
    groups, span = base.shape
    length, channels = ext.shape
    half = rows // 2
    assert rows % 32 == 0 and half + span <= length and span >= half + LANES - 1
    gb = groups * LANES // channels
    steps = channels // LANES
    flops = 4 * half * span * 2 * LANES * gb * steps
    return pl.pallas_call(
        _toeplitz_kernel,
        grid=(steps,),
        in_specs=[
            pl.BlockSpec((gb, span), lambda i: (i, 0)),
            pl.BlockSpec((length, LANES), lambda i: (0, i)),
        ],
        out_specs=pl.BlockSpec((rows, LANES), lambda i: (0, i)),
        out_shape=jax.ShapeDtypeStruct((rows, channels), jnp.float32),
        cost_estimate=pl.CostEstimate(
            flops=flops, transcendentals=0,
            bytes_accessed=4 * (base.size + ext.size + rows * channels)),
    )(base, ext)


def shift_perm(n, step):
    if step > 0:
        return [(j, j + 1) for j in range(n - 1)]
    return [(j + 1, j) for j in range(n - 1)]


def block(projected, feat_taps, filters, out_weight, cotangent):
    rows = projected.shape[0]
    feat_len = feat_taps.shape[0]
    filt_len = filters.shape[1]
    channels = projected.shape[2]
    n = lax.axis_size("seq")
    fwd = shift_perm(n, 1)
    bwd = shift_perm(n, -1)
    fh = feat_len - 1
    lh = filt_len - 1
    reach = lh + fh
    assert reach <= rows
    ext_len = -(-(rows + reach) // LANES) * LANES
    fwd_rows = rows
    bwd_rows = -(-(rows + fh) // 32) * 32
    span_f = -(-(fwd_rows // 2 + lh) // LANES) * LANES
    span_b = -(-(bwd_rows // 2 + lh) // LANES) * LANES
    base_fwd = jnp.pad(filters[:, ::-1], ((0, 0), (0, span_f - filt_len))).astype(jnp.bfloat16)
    base_bwd = jnp.pad(filters, ((0, 0), (0, span_b - filt_len))).astype(jnp.bfloat16)
    base_fwd = base_fwd.astype(jnp.float32)
    base_bwd = base_bwd.astype(jnp.float32)

    prev_proj = lax.ppermute(projected[rows - fh:], "seq", fwd)
    next_proj = lax.ppermute(projected[:fh], "seq", bwd)
    ext = jnp.concatenate([prev_proj, projected, next_proj], axis=0)

    def featurize(stream, out_rows):
        sig = ext[:, stream].astype(jnp.float32)
        out = feat_taps[0, stream] * sig[fh:fh + out_rows]
        for d in range(1, feat_len):
            out = out + feat_taps[d, stream] * sig[fh - d:fh - d + out_rows]
        return out

    query = featurize(0, rows)
    key_ext = featurize(1, rows + fh)
    value_ext = featurize(2, rows + fh)
    key_feat = key_ext[:rows]
    value_feat = value_ext[:rows]
    product = key_feat * value_feat

    prev_prod = lax.ppermute(product[rows - lh:], "seq", fwd)
    pext = jnp.concatenate(
        [prev_prod, product, jnp.zeros((ext_len - rows - lh, channels), jnp.float32)], axis=0
    )
    conv = toeplitz_conv(base_fwd, pext, fwd_rows)
    mixed = (query * conv).astype(jnp.bfloat16)

    n_tp = lax.axis_size("tp")
    weight_blocks = out_weight.reshape(channels, n_tp, out_weight.shape[1] // n_tp)
    partial = jnp.einsum(
        "tc,cbd->btd", mixed, weight_blocks, preferred_element_type=jnp.float32
    ).astype(jnp.bfloat16)
    output = lax.psum_scatter(partial, "tp", scatter_dimension=0, tiled=False)

    query, key_ext, value_ext, conv = lax.optimization_barrier(
        (query, key_ext, value_ext, conv)
    )
    cot_blocks = lax.all_gather(cotangent, "tp", axis=0, tiled=False)
    grad_mixed = jnp.einsum(
        "bte,cbe->tc", cot_blocks, weight_blocks, preferred_element_type=jnp.float32
    )
    signal_grad = grad_mixed * query
    query_grad = grad_mixed * conv
    next_sig, next_qg = lax.ppermute((signal_grad[:reach], query_grad[:fh]), "seq", bwd)
    sext = jnp.concatenate(
        [signal_grad, next_sig, jnp.zeros((ext_len - rows - reach, channels), jnp.float32)], axis=0
    )
    conv_grad = toeplitz_conv(base_bwd, sext, bwd_rows)[:rows + fh]
    qg_ext = jnp.concatenate([query_grad, next_qg], axis=0)
    dext = jnp.stack([qg_ext, conv_grad * value_ext, conv_grad * key_ext], axis=1)
    igrad = feat_taps[0] * dext[:rows]
    for d in range(1, feat_len):
        igrad = igrad + feat_taps[d] * dext[d:d + rows]
    return output, igrad.astype(jnp.bfloat16)


def solution(mesh):
    in_specs = (
        P("seq", None, "tp"),
        P(None, None, "tp"),
        P("tp", None),
        P("tp", None),
        P("seq", "tp"),
    )
    out_specs = (P("seq", "tp"), P("seq", None, "tp"))
    return jax.shard_map(block, mesh=mesh, in_specs=in_specs, out_specs=out_specs, check_vma=False)
```

```python
import jax
import jax.numpy as jnp
from jax import lax
from jax.experimental import pallas as pl
from jax.experimental.pallas import tpu as pltpu
from jax.sharding import PartitionSpec as P

LANES = 128


def _toeplitz_kernel(*refs):
    base_ref, *part_refs, out_ref = refs
    gb, span = base_ref.shape
    rows, width = out_ref.shape
    half = rows // 2
    hg = width // gb
    pieces = [r[...] for r in part_refs]
    filled = sum(x.shape[0] for x in pieces)
    need = half + span
    if filled < need:
        pieces.append(jnp.zeros((need - filled, width), jnp.float32))
    p = jnp.concatenate(pieces, axis=0)
    p2 = jnp.concatenate([p[:span], p[half:half + span]], axis=1)
    p_hi = p2.astype(jnp.bfloat16)
    p_lo = (p2 - p_hi.astype(jnp.float32)).astype(jnp.bfloat16)
    lane_group = (lax.broadcasted_iota(jnp.int32, (half, 2 * width), 1) % width) // hg
    acc = jnp.zeros((half, 2 * width), jnp.float32)
    for g in range(gb):
        t = jnp.broadcast_to(base_ref[pl.ds(g, 1), :], (half, span))
        t = pltpu.roll(t, 0, 1, stride=1, stride_axis=0).astype(jnp.bfloat16)
        res = jnp.dot(t, p_hi, preferred_element_type=jnp.float32)
        res = res + jnp.dot(t, p_lo, preferred_element_type=jnp.float32)
        acc = jnp.where(lane_group == g, res, acc)
    out_ref[pl.ds(0, half), :] = acc[:, :width]
    out_ref[pl.ds(half, half), :] = acc[:, width:]


def toeplitz_conv(base, parts, rows):
    groups, span = base.shape
    channels = parts[0].shape[1]
    half = rows // 2
    assert rows % 32 == 0 and all(x.shape[0] % 8 == 0 for x in parts)
    assert sum(x.shape[0] for x in parts) <= half + span
    gb = groups * LANES // channels
    steps = channels // LANES
    flops = 4 * half * span * 2 * LANES * gb * steps
    in_specs = [pl.BlockSpec((gb, span), lambda i: (i, 0))]
    in_specs += [pl.BlockSpec((x.shape[0], LANES), lambda i: (0, i)) for x in parts]
    return pl.pallas_call(
        _toeplitz_kernel,
        grid=(steps,),
        in_specs=in_specs,
        out_specs=pl.BlockSpec((rows, LANES), lambda i: (0, i)),
        out_shape=jax.ShapeDtypeStruct((rows, channels), jnp.float32),
        cost_estimate=pl.CostEstimate(
            flops=flops, transcendentals=0,
            bytes_accessed=4 * (base.size + sum(x.size for x in parts) + rows * channels)),
    )(base, *parts)


def shift_perm(n, step):
    if step > 0:
        return [(j, j + 1) for j in range(n - 1)]
    return [(j + 1, j) for j in range(n - 1)]


def block(projected, feat_taps, filters, out_weight, cotangent):
    rows = projected.shape[0]
    feat_len = feat_taps.shape[0]
    filt_len = filters.shape[1]
    n = lax.axis_size("seq")
    fwd = shift_perm(n, 1)
    bwd = shift_perm(n, -1)
    fh = feat_len - 1
    lh = filt_len - 1
    reach = lh + fh
    assert reach <= rows
    fwd_rows = rows
    bwd_rows = -(-(rows + fh) // 32) * 32
    span_f = -(-(fwd_rows // 2 + filt_len) // LANES) * LANES
    halo_f = -(-filt_len // 8) * 8
    halo_b = -(-reach // 8) * 8
    span_b = -(-(bwd_rows // 2 + lh) // LANES) * LANES
    base_fwd = jnp.pad(filters[:, ::-1], ((0, 0), (halo_f - filt_len + 1, span_f - halo_f - 1))).astype(jnp.bfloat16)
    base_bwd = jnp.pad(filters, ((0, 0), (0, span_b - filt_len))).astype(jnp.bfloat16)
    base_fwd = base_fwd.astype(jnp.float32)
    base_bwd = base_bwd.astype(jnp.float32)

    prev_proj = lax.ppermute(projected[rows - fh:], "seq", fwd)
    next_proj = lax.ppermute(projected[:fh], "seq", bwd)
    ext = jnp.concatenate([prev_proj, projected, next_proj], axis=0)

    def featurize(stream, out_rows):
        sig = ext[:, stream].astype(jnp.float32)
        out = feat_taps[0, stream] * sig[fh:fh + out_rows]
        for d in range(1, feat_len):
            out = out + feat_taps[d, stream] * sig[fh - d:fh - d + out_rows]
        return out

    query = featurize(0, rows)
    key_ext = featurize(1, rows + fh)
    value_ext = featurize(2, rows + fh)
    key_feat = key_ext[:rows]
    value_feat = value_ext[:rows]
    product = key_feat * value_feat

    prev_prod = lax.ppermute(product[rows - halo_f:], "seq", fwd)
    conv = toeplitz_conv(base_fwd, [prev_prod, product], fwd_rows)
    mixed = (query * conv).astype(jnp.bfloat16)

    partial = jnp.einsum(
        "tc,cd->td", mixed, out_weight, preferred_element_type=jnp.float32
    ).astype(jnp.bfloat16)
    output = lax.psum_scatter(partial, "tp", scatter_dimension=1, tiled=True)

    query, key_ext, value_ext, conv = lax.optimization_barrier(
        (query, key_ext, value_ext, conv)
    )
    cot_full = lax.all_gather(cotangent, "tp", axis=1, tiled=True)
    grad_mixed = jnp.einsum(
        "te,ce->tc", cot_full, out_weight, preferred_element_type=jnp.float32
    )
    signal_grad = grad_mixed * query
    query_grad = grad_mixed * conv
    next_sig, next_qg = lax.ppermute((signal_grad[:halo_b], query_grad[:fh]), "seq", bwd)
    conv_grad = toeplitz_conv(base_bwd, [signal_grad, next_sig], bwd_rows)[:rows + fh]
    qg_ext = jnp.concatenate([query_grad, next_qg], axis=0)
    dext = jnp.stack([qg_ext, conv_grad * value_ext, conv_grad * key_ext], axis=1)
    igrad = feat_taps[0] * dext[:rows]
    for d in range(1, feat_len):
        igrad = igrad + feat_taps[d] * dext[d:d + rows]
    return output, igrad.astype(jnp.bfloat16)


def solution(mesh):
    in_specs = (
        P("seq", None, "tp"),
        P(None, None, "tp"),
        P("tp", None),
        P("tp", None),
        P("seq", "tp"),
    )
    out_specs = (P("seq", "tp"), P("seq", None, "tp"))
    return jax.shard_map(block, mesh=mesh, in_specs=in_specs, out_specs=out_specs, check_vma=False)
```

```python
import jax
import jax.numpy as jnp
from jax import lax
from jax.experimental import pallas as pl
from jax.experimental.pallas import tpu as pltpu
from jax.sharding import PartitionSpec as P

LANES = 128


def _toeplitz_kernel(base_ref, ext_ref, out_ref):
    gb, span = base_ref.shape
    rows, width = out_ref.shape
    half = rows // 2
    hg = width // gb
    p = ext_ref[...]
    p2 = jnp.concatenate([p[:span], p[half:half + span]], axis=1)
    p_hi = p2.astype(jnp.bfloat16)
    p_lo = (p2 - p_hi.astype(jnp.float32)).astype(jnp.bfloat16)
    lane_group = (lax.broadcasted_iota(jnp.int32, (half, 2 * width), 1) % width) // hg
    acc = jnp.zeros((half, 2 * width), jnp.float32)
    for g in range(gb):
        t = jnp.broadcast_to(base_ref[pl.ds(g, 1), :], (half, span))
        t = pltpu.roll(t, 0, 1, stride=1, stride_axis=0)
        t_hi = t.astype(jnp.bfloat16)
        t_lo = (t - t_hi.astype(jnp.float32)).astype(jnp.bfloat16)
        res = jnp.dot(t_hi, p_hi, preferred_element_type=jnp.float32)
        res = res + jnp.dot(t_hi, p_lo, preferred_element_type=jnp.float32)
        res = res + jnp.dot(t_lo, p_hi, preferred_element_type=jnp.float32)
        acc = jnp.where(lane_group == g, res, acc)
    out_ref[pl.ds(0, half), :] = acc[:, :width]
    out_ref[pl.ds(half, half), :] = acc[:, width:]


def toeplitz_conv(base, ext, rows):
    groups, span = base.shape
    length, channels = ext.shape
    half = rows // 2
    assert rows % 32 == 0 and half + span <= length and span >= half + LANES - 1
    gb = groups * LANES // channels
    steps = channels // LANES
    flops = 6 * half * span * 2 * LANES * gb * steps
    return pl.pallas_call(
        _toeplitz_kernel,
        grid=(steps,),
        in_specs=[
            pl.BlockSpec((gb, span), lambda i: (i, 0)),
            pl.BlockSpec((length, LANES), lambda i: (0, i)),
        ],
        out_specs=pl.BlockSpec((rows, LANES), lambda i: (0, i)),
        out_shape=jax.ShapeDtypeStruct((rows, channels), jnp.float32),
        cost_estimate=pl.CostEstimate(
            flops=flops, transcendentals=0,
            bytes_accessed=4 * (base.size + ext.size + rows * channels)),
    )(base, ext)


def shift_perm(n, step):
    if step > 0:
        return [(j, j + 1) for j in range(n - 1)]
    return [(j + 1, j) for j in range(n - 1)]


def block(projected, feat_taps, filters, out_weight, cotangent):
    rows = projected.shape[0]
    feat_len = feat_taps.shape[0]
    filt_len = filters.shape[1]
    channels = projected.shape[2]
    n = lax.axis_size("seq")
    fwd = shift_perm(n, 1)
    bwd = shift_perm(n, -1)
    fh = feat_len - 1
    lh = filt_len - 1
    reach = lh + fh
    assert reach <= rows
    ext_len = -(-(rows + reach) // LANES) * LANES
    fwd_rows = rows
    bwd_rows = -(-(rows + fh) // 32) * 32
    span_f = -(-(fwd_rows // 2 + lh) // LANES) * LANES
    span_b = -(-(bwd_rows // 2 + lh) // LANES) * LANES
    base_fwd = jnp.pad(filters[:, ::-1], ((0, 0), (0, span_f - filt_len)))
    base_bwd = jnp.pad(filters, ((0, 0), (0, span_b - filt_len)))

    prev_proj = lax.ppermute(projected[rows - fh:], "seq", fwd)
    next_proj = lax.ppermute(projected[:fh], "seq", bwd)
    ext = jnp.concatenate([prev_proj, projected, next_proj], axis=0)

    def featurize(stream, out_rows):
        sig = ext[:, stream].astype(jnp.float32)
        out = feat_taps[0, stream] * sig[fh:fh + out_rows]
        for d in range(1, feat_len):
            out = out + feat_taps[d, stream] * sig[fh - d:fh - d + out_rows]
        return out

    query = featurize(0, rows)
    key_ext = featurize(1, rows + fh)
    value_ext = featurize(2, rows + fh)
    key_feat = key_ext[:rows]
    value_feat = value_ext[:rows]
    product = key_feat * value_feat

    prev_prod = lax.ppermute(product[rows - lh:], "seq", fwd)
    pext = jnp.concatenate(
        [prev_prod, product, jnp.zeros((ext_len - rows - lh, channels), jnp.float32)], axis=0
    )
    conv = toeplitz_conv(base_fwd, pext, fwd_rows)
    mixed = (query * conv).astype(jnp.bfloat16)

    partial = jnp.einsum(
        "tc,cd->td", mixed, out_weight, preferred_element_type=jnp.float32
    ).astype(jnp.bfloat16)
    output = lax.psum_scatter(partial, "tp", scatter_dimension=1, tiled=True)

    query, key_ext, value_ext, conv = lax.optimization_barrier(
        (query, key_ext, value_ext, conv)
    )
    cot_full = lax.all_gather(cotangent, "tp", axis=1, tiled=True)
    grad_mixed = jnp.einsum(
        "te,ce->tc", cot_full, out_weight, preferred_element_type=jnp.float32
    )
    signal_grad = grad_mixed * query
    query_grad = grad_mixed * conv
    next_sig, next_qg = lax.ppermute((signal_grad[:reach], query_grad[:fh]), "seq", bwd)
    sext = jnp.concatenate(
        [signal_grad, next_sig, jnp.zeros((ext_len - rows - reach, channels), jnp.float32)], axis=0
    )
    conv_grad = toeplitz_conv(base_bwd, sext, bwd_rows)[:rows + fh]
    qg_ext = jnp.concatenate([query_grad, next_qg], axis=0)
    dext = jnp.stack([qg_ext, conv_grad * value_ext, conv_grad * key_ext], axis=1)
    igrad = feat_taps[0] * dext[:rows]
    for d in range(1, feat_len):
        igrad = igrad + feat_taps[d] * dext[d:d + rows]
    return output, igrad.astype(jnp.bfloat16)


def solution(mesh):
    in_specs = (
        P("seq", None, "tp"),
        P(None, None, "tp"),
        P("tp", None),
        P("tp", None),
        P("seq", "tp"),
    )
    out_specs = (P("seq", "tp"), P("seq", None, "tp"))
    return jax.shard_map(block, mesh=mesh, in_specs=in_specs, out_specs=out_specs, check_vma=False)
```
